256 devices in a mesh: night: 4 (over y_lo, core), bl: 64 (over x, y_hi, z).
Axes of the slice: x: 4, y: 4 (y_hi: 2, y_lo: 2; y = y_hi * 2 + y_lo), z: 8, core: 2. Of those that a mesh axis runs over, the one named last changes fastest.
Arguments:
- visibility: bfloat16 [8, 64, 512, 2, 1536], P('night', 'bl'), may hold values from -6 to 6
- delay_filter: bfloat16 [1536, 1536], replicated, may hold values from -0.15625 to 0.15625
- fringe_taps: float32 [512, 2, 31], P('bl'), may hold values from -0.8 to 0.8
- lst_bin: int32 [8, 64], P('night'), may hold values from 0 to 79, as said below
- flag_mask: int32 [8, 64, 512], P('night', None, 'bl'), may hold values 0 or 1
Outputs:
- lst_mean: float32 [80, 512, 2, 1536], P('night', 'bl')
- lst_count: float32 [80, 512], P('night', 'bl')
The draws below stay inside these ranges and needn't reach their ends.
Inputs may be any that keep to these rules, and one draw needn't show every extreme that they name: Each night covers consecutive bins: lst_bin[n, t] = lst_bin[n, 0] + t. Some night starts at bin 0 and another at bin 16.
All inputs are finite; a program needn't handle non-finite values. No bound on the sum of `flag_mask` on one device may be relied on, other than what follows from the above.
Results may differ from the reference program's by a relative error of at most 0.007.
Values may be sent and summed in bfloat16 or wider, within the bound.
No kernel may reach another device: no remote copies, remote signals or barrier semaphores. Data moves between devices by JAX's collectives and lax.ppermute only.
A program may use at most 128 MiB of HBM per device.

```python
import jax
import jax.numpy as jnp
from jax import lax

CH = 1536
TIMES = 64
TAPS = 31
SPREAD = 16
NIGHTS = 8
BL = 512
NBINS = 80


def draw_lst_bin(key, part):
    base_key = jax.random.fold_in(key, 7919)
    start_key, order_key = jax.random.split(base_key)
    offsets = jax.random.randint(start_key, (NIGHTS,), 0, SPREAD + 1)
    order = jax.random.permutation(order_key, NIGHTS)
    offsets = offsets.at[order[0]].set(0).at[order[1]].set(SPREAD)
    return (offsets[:, None] + jnp.arange(TIMES)[None, :]).astype(jnp.int32)


def plant(array, stream_key, least, top_value):
    longest = array.shape.index(max(array.shape))
    spots = []
    for shift in (0, 1):
        where = [jax.random.randint(jax.random.fold_in(stream_key, axis), (), 0, length) for axis, length in enumerate(array.shape)]
        where[longest] = (where[longest] + shift) % array.shape[longest]
        spots.append(tuple(where))
    return array.at[spots[0]].set(least).at[spots[1]].set(top_value)


def steps_of(key, shape, cuts, smallest, high):
    factor_of, own = 1.0, jax.random.fold_in(key, 6)
    for axis_at, parts in cuts:
        steps = jnp.exp(jax.random.uniform(jax.random.fold_in(own, axis_at), (parts,), jnp.float32, smallest / len(cuts), high / len(cuts)))
        factor_of = factor_of * jnp.repeat(steps, shape[axis_at] // parts).reshape([-1 if axis == axis_at else 1 for axis in range(len(shape))])
    return factor_of


def centred(key, extent, deviation, most, cuts=(), held_as=jnp.bfloat16):
    loudness = steps_of(key, extent, cuts, -0.22, 0.18) if cuts else 1.0
    values = jax.random.normal(key, extent, jnp.float32) * deviation * loudness
    return jnp.minimum(jnp.maximum(values, -most), most).astype(held_as)


def setup_inputs(seed: int = 0) -> dict:
    streams_of = jax.random.split(jax.random.key(seed), 6)
    visibility = centred(streams_of[0], (NIGHTS, TIMES, BL, 2, CH), 1.0, 6.0, ((0, 4), (1, 64)))
    delay_filter = centred(streams_of[1], (CH, CH), CH ** -0.5, 0.15625)
    fringe_taps = centred(streams_of[2], (BL, 2, TAPS), 0.13, 0.8, ((0, 64),), jnp.float32)
    lst_bin = draw_lst_bin(jax.random.fold_in(streams_of[5], 71), 0)
    flag_mask = plant((jax.random.randint(streams_of[4], (NIGHTS, TIMES, BL), 0, 8) < 7).astype(jnp.int32), jax.random.fold_in(streams_of[4], 1), 0, 1)
    return {"visibility": visibility, "delay_filter": delay_filter, "fringe_taps": fringe_taps, "lst_bin": lst_bin, "flag_mask": flag_mask}


def reference(visibility, delay_filter, fringe_taps, lst_bin, flag_mask):
    half_taps = TAPS // 2
    total_bl = visibility.shape[2]

    def one_night(totals, inputs):
        vis_night, bins_night, flag_night = inputs
        product = jnp.dot(vis_night.reshape(-1, CH), delay_filter, preferred_element_type=jnp.float32)
        filtered = product.astype(jnp.bfloat16).reshape(vis_night.shape)
        filtered = filtered * flag_night.astype(jnp.bfloat16)[:, :, None, None]
        night_rows = filtered.astype(jnp.float32)
        padded = jnp.pad(night_rows, ((half_taps, half_taps), (0, 0), (0, 0), (0, 0)))
        real_part = jnp.zeros((TIMES, total_bl, CH), jnp.float32)
        imag_part = jnp.zeros((TIMES, total_bl, CH), jnp.float32)
        for tap_idx in range(TAPS):
            shifted = padded[tap_idx:tap_idx + TIMES]
            tap_real = fringe_taps[:, 0, tap_idx][None, :, None]
            tap_imag = fringe_taps[:, 1, tap_idx][None, :, None]
            real_part = real_part + tap_real * shifted[:, :, 0] - tap_imag * shifted[:, :, 1]
            imag_part = imag_part + tap_real * shifted[:, :, 1] + tap_imag * shifted[:, :, 0]
        smoothed = jnp.stack([real_part, imag_part], axis=2)
        lst_sums = totals[0] + jax.ops.segment_sum(smoothed, bins_night, num_segments=NBINS)
        counts = totals[1] + jax.ops.segment_sum(flag_night.astype(jnp.float32), bins_night, num_segments=NBINS)
        return (lst_sums, counts), None

    start_sums = jnp.zeros((NBINS, total_bl, 2, CH), jnp.float32)
    start_counts = jnp.zeros((NBINS, total_bl), jnp.float32)
    (lst_sums, counts), unused = lax.scan(one_night, (start_sums, start_counts), (visibility, lst_bin, flag_mask))
    lst_mean = lst_sums / jnp.maximum(counts, 1.0)[:, :, None, None]
    return lst_mean, counts
```

```python
import jax
import jax.numpy as jnp
from jax import lax
from jax.sharding import PartitionSpec as P

NBINS = 80
CHUNKS = 4


def smoothing_matrix(fringe_taps, lst_bin, flag_mask):
    nights = lst_bin.shape[0]
    times = lst_bin.shape[1]
    taps = fringe_taps.shape[2]
    half_taps = taps // 2
    start = lst_bin[:, 0]
    j = jnp.arange(NBINS, dtype=jnp.int32)[:, None, None]
    s = jnp.arange(times, dtype=jnp.int32)[None, None, :]
    t = j - start[None, :, None]
    k = s - t + half_taps
    inside = (t >= 0) & (t < times)
    onehot = ((k[..., None] == jnp.arange(taps, dtype=jnp.int32)) & inside[..., None]).astype(jnp.float32)
    h = jnp.einsum("jnsk,bqk->bqjns", onehot, fringe_taps, precision=lax.Precision.HIGHEST)
    hr = h[:, 0]
    hi = h[:, 1]
    row_real = jnp.stack([hr, -hi], axis=3)
    row_imag = jnp.stack([hi, hr], axis=3)
    w = jnp.stack([row_real, row_imag], axis=1)
    flags = jnp.transpose(flag_mask.astype(jnp.float32), (2, 0, 1))
    w = w * flags[:, None, None, :, None, :]
    return w


def per_device(visibility, delay_filter, fringe_taps, lst_bin, flag_mask):
    nights, _, total_bl, parts, channels = visibility.shape
    width = channels // CHUNKS
    rows = visibility.reshape(-1, channels)
    w = smoothing_matrix(fringe_taps, lst_bin, flag_mask)
    w_high = w.astype(jnp.bfloat16)
    w_low = (w - w_high.astype(jnp.float32)).astype(jnp.bfloat16)

    times = lst_bin.shape[1]
    j = jnp.arange(NBINS, dtype=jnp.int32)[:, None, None]
    s = jnp.arange(times, dtype=jnp.int32)[None, None, :]
    place = (j - lst_bin[:, 0][None, :, None] == s).astype(jnp.float32)
    partial_count = jnp.einsum("jns,nsb->jb", place, flag_mask.astype(jnp.float32),
                               precision=lax.Precision.HIGHEST)
    counts = lax.psum_scatter(partial_count, "night", scatter_dimension=0, tiled=True)
    divisor = jnp.maximum(counts, 1.0)[:, :, None, None]

    pieces = []
    for c in range(CHUNKS):
        filt = lax.slice_in_dim(delay_filter, c * width, (c + 1) * width, axis=1)
        product = jnp.dot(rows, filt, preferred_element_type=jnp.float32).astype(jnp.bfloat16)
        product = product.reshape(nights, 1, total_bl, parts, width)
        moved = lax.all_to_all(product, "bl", split_axis=2, concat_axis=1, tiled=True)
        sums = jnp.einsum("bojnps,nsbpc->jboc", w_high, moved, preferred_element_type=jnp.float32)
        sums = sums + jnp.einsum("bojnps,nsbpc->jboc", w_low, moved, preferred_element_type=jnp.float32)
        lst_sums = lax.psum_scatter(sums, "night", scatter_dimension=0, tiled=True)
        pieces.append(lst_sums / divisor)
    lst_mean = jnp.concatenate(pieces, axis=3)
    return (lst_mean, counts)


def solution(mesh):
    in_specs = (
        P("night", "bl", None, None, None),
        P(),
        P("bl", None, None),
        P("night", None),
        P("night", None, "bl"),
    )
    out_specs = (P("night", "bl", None, None), P("night", "bl"))
    return jax.shard_map(
        per_device, mesh=mesh, in_specs=in_specs, out_specs=out_specs, check_vma=False
    )
```

```python
import jax
import jax.numpy as jnp
from jax import lax
from jax.sharding import PartitionSpec as P

NBINS = 80


def smoothing_matrix(fringe_taps, lst_bin, flag_mask):
    nights = lst_bin.shape[0]
    times = lst_bin.shape[1]
    taps = fringe_taps.shape[2]
    half_taps = taps // 2
    start = lst_bin[:, 0]
    j = jnp.arange(NBINS, dtype=jnp.int32)[:, None, None]
    s = jnp.arange(times, dtype=jnp.int32)[None, None, :]
    t = j - start[None, :, None]
    k = s - t + half_taps
    inside = (t >= 0) & (t < times)
    onehot = ((k[..., None] == jnp.arange(taps, dtype=jnp.int32)) & inside[..., None]).astype(jnp.float32)
    h = jnp.einsum("jnsk,bqk->bqjns", onehot, fringe_taps, precision=lax.Precision.HIGHEST)
    hr = h[:, 0]
    hi = h[:, 1]
    row_real = jnp.stack([hr, -hi], axis=3)
    row_imag = jnp.stack([hi, hr], axis=3)
    w = jnp.stack([row_real, row_imag], axis=1)
    flags = jnp.transpose(flag_mask.astype(jnp.float32), (2, 0, 1))
    w = w * flags[:, None, None, :, None, :]
    return w


def per_device(visibility, delay_filter, fringe_taps, lst_bin, flag_mask):
    nights, _, total_bl, parts, channels = visibility.shape
    groups = lax.psum(1, "night")
    bl_size = lax.psum(1, "bl")
    group = lax.axis_index("night")
    per_dest = total_bl // (groups * bl_size)
    local_bl = flag_mask.shape[2]

    product = jnp.dot(visibility.reshape(-1, channels), delay_filter,
                      preferred_element_type=jnp.float32).astype(jnp.bfloat16)
    product = product.reshape(nights, bl_size, groups, per_dest, parts, channels)
    product = jnp.transpose(product, (2, 1, 0, 3, 4, 5))
    product = product.reshape(groups * bl_size, nights, per_dest, parts, channels)
    moved = lax.all_to_all(product, ("night", "bl"), split_axis=0, concat_axis=0, tiled=True)
    moved = moved.reshape(groups, bl_size, nights, per_dest, parts, channels)

    all_bins = lax.all_gather(lst_bin, "night", axis=0, tiled=True)
    all_flags = lax.all_gather(flag_mask, "night", axis=0, tiled=True)
    own_flags = lax.dynamic_slice_in_dim(all_flags, group * per_dest, per_dest, axis=2)
    own_taps = lax.dynamic_slice_in_dim(fringe_taps, group * per_dest, per_dest, axis=0)
    w = smoothing_matrix(own_taps, all_bins, own_flags)
    w = w.reshape(per_dest, parts, NBINS, groups, nights, parts, bl_size)
    w_high = w.astype(jnp.bfloat16)
    w_low = (w - w_high.astype(jnp.float32)).astype(jnp.bfloat16)
    sums = jnp.einsum("bojgnps,gsnbpc->jboc", w_high, moved, preferred_element_type=jnp.float32)
    sums = sums + jnp.einsum("bojgnps,gsnbpc->jboc", w_low, moved, preferred_element_type=jnp.float32)
    lst_sums = lax.all_to_all(sums, "night", split_axis=0, concat_axis=1, tiled=True)

    times = all_bins.shape[1]
    j = jnp.arange(NBINS, dtype=jnp.int32)[:, None, None]
    s = jnp.arange(times, dtype=jnp.int32)[None, None, :]
    place = (j - all_bins[:, 0][None, :, None] == s).astype(jnp.float32)
    full_count = jnp.einsum("jns,nsb->jb", place, all_flags.astype(jnp.float32),
                            precision=lax.Precision.HIGHEST)
    block = NBINS // groups
    counts = lax.dynamic_slice_in_dim(full_count, group * block, block, axis=0)
    lst_mean = lst_sums / jnp.maximum(counts, 1.0)[:, :, None, None]
    return (lst_mean, counts)


def solution(mesh):
    in_specs = (
        P("night", "bl", None, None, None),
        P(),
        P("bl", None, None),
        P("night", None),
        P("night", None, "bl"),
    )
    out_specs = (P("night", "bl", None, None), P("night", "bl"))
    return jax.shard_map(
        per_device, mesh=mesh, in_specs=in_specs, out_specs=out_specs, check_vma=False
    )
```

```python
import jax
import jax.numpy as jnp
from jax import lax
from jax.sharding import PartitionSpec as P

NBINS = 80


def smoothing_matrix(fringe_taps, lst_bin, flag_mask):
    nights = lst_bin.shape[0]
    times = lst_bin.shape[1]
    taps = fringe_taps.shape[2]
    half_taps = taps // 2
    start = lst_bin[:, 0]
    j = jnp.arange(NBINS, dtype=jnp.int32)[:, None, None]
    s = jnp.arange(times, dtype=jnp.int32)[None, None, :]
    t = j - start[None, :, None]
    k = s - t + half_taps
    inside = (t >= 0) & (t < times)
    onehot = ((k[..., None] == jnp.arange(taps, dtype=jnp.int32)) & inside[..., None]).astype(jnp.float32)
    h = jnp.einsum("jnsk,bqk->bqjns", onehot, fringe_taps, precision=lax.Precision.HIGHEST)
    hr = h[:, 0]
    hi = h[:, 1]
    row_real = jnp.stack([hr, -hi], axis=3)
    row_imag = jnp.stack([hi, hr], axis=3)
    w = jnp.stack([row_real, row_imag], axis=1)
    flags = jnp.transpose(flag_mask.astype(jnp.float32), (2, 0, 1))
    w = w * flags[:, None, None, :, None, :]
    return w


def per_device(visibility, delay_filter, fringe_taps, lst_bin, flag_mask):
    nights, _, total_bl, parts, channels = visibility.shape
    groups = lax.psum(1, "night")
    bl_size = lax.psum(1, "bl")
    group = lax.axis_index("night")
    per_dest = total_bl // (groups * bl_size)

    moved = lax.all_to_all(visibility, ("bl", "night"), split_axis=2, concat_axis=1, tiled=True)
    filtered = jnp.einsum("ntbpc,cd->ntbpd", moved, delay_filter,
                          preferred_element_type=jnp.float32).astype(jnp.bfloat16)
    filtered = filtered.reshape(nights, bl_size, groups, per_dest, parts, channels)

    all_bins = lax.all_gather(lst_bin, "night", axis=0, tiled=True)
    all_flags = lax.all_gather(flag_mask, "night", axis=0, tiled=True)
    own_flags = lax.dynamic_slice_in_dim(all_flags, group * per_dest, per_dest, axis=2)
    own_taps = lax.dynamic_slice_in_dim(fringe_taps, group * per_dest, per_dest, axis=0)
    w = smoothing_matrix(own_taps, all_bins, own_flags)
    w = w.reshape(per_dest, parts, NBINS, groups, nights, parts, bl_size)
    w_high = w.astype(jnp.bfloat16)
    w_low = (w - w_high.astype(jnp.float32)).astype(jnp.bfloat16)
    sums = jnp.einsum("bojgnps,nsgbpc->jboc", w_high, filtered, preferred_element_type=jnp.float32)
    sums = sums + jnp.einsum("bojgnps,nsgbpc->jboc", w_low, filtered, preferred_element_type=jnp.float32)
    lst_sums = lax.all_to_all(sums, "night", split_axis=0, concat_axis=1, tiled=True)

    times = all_bins.shape[1]
    j = jnp.arange(NBINS, dtype=jnp.int32)[:, None, None]
    s = jnp.arange(times, dtype=jnp.int32)[None, None, :]
    place = (j - all_bins[:, 0][None, :, None] == s).astype(jnp.float32)
    full_count = jnp.einsum("jns,nsb->jb", place, all_flags.astype(jnp.float32),
                            precision=lax.Precision.HIGHEST)
    block = NBINS // groups
    counts = lax.dynamic_slice_in_dim(full_count, group * block, block, axis=0)
    lst_mean = lst_sums / jnp.maximum(counts, 1.0)[:, :, None, None]
    return (lst_mean, counts)


def solution(mesh):
    in_specs = (
        P("night", "bl", None, None, None),
        P(),
        P("bl", None, None),
        P("night", None),
        P("night", None, "bl"),
    )
    out_specs = (P("night", "bl", None, None), P("night", "bl"))
    return jax.shard_map(
        per_device, mesh=mesh, in_specs=in_specs, out_specs=out_specs, check_vma=False
    )
```

```python
import jax
import jax.numpy as jnp
from jax import lax
from jax.sharding import PartitionSpec as P

NBINS = 80


def smoothing_matrix(fringe_taps, lst_bin, flag_mask):
    nights = lst_bin.shape[0]
    times = lst_bin.shape[1]
    taps = fringe_taps.shape[2]
    half_taps = taps // 2
    start = lst_bin[:, 0]
    j = jnp.arange(NBINS, dtype=jnp.int32)[:, None, None]
    s = jnp.arange(times, dtype=jnp.int32)[None, None, :]
    t = j - start[None, :, None]
    k = s - t + half_taps
    inside = (t >= 0) & (t < times)
    onehot = ((k[..., None] == jnp.arange(taps, dtype=jnp.int32)) & inside[..., None]).astype(jnp.float32)
    h = jnp.einsum("jnsk,bqk->bqjns", onehot, fringe_taps, precision=lax.Precision.HIGHEST)
    hr = h[:, 0]
    hi = h[:, 1]
    row_real = jnp.stack([hr, -hi], axis=3)
    row_imag = jnp.stack([hi, hr], axis=3)
    w = jnp.stack([row_real, row_imag], axis=1)
    flags = jnp.transpose(flag_mask.astype(jnp.float32), (2, 0, 1))
    w = w * flags[:, None, None, :, None, :]
    return w


def per_device(visibility, delay_filter, fringe_taps, lst_bin, flag_mask):
    nights, _, total_bl, parts, channels = visibility.shape
    groups = lax.psum(1, "night")
    bl_size = lax.psum(1, "bl")
    group = lax.axis_index("night")
    per_dest = total_bl // (groups * bl_size)

    all_bins = lax.all_gather(lst_bin, "night", axis=0, tiled=True)
    all_flags = lax.all_gather(flag_mask, "night", axis=0, tiled=True)
    own_flags = lax.dynamic_slice_in_dim(all_flags, group * per_dest, per_dest, axis=2)
    own_taps = lax.dynamic_slice_in_dim(fringe_taps, group * per_dest, per_dest, axis=0)
    w = smoothing_matrix(own_taps, all_bins, own_flags)
    w = w.reshape(per_dest, parts, NBINS, groups, nights, parts, bl_size)
    w = jnp.transpose(w, (0, 1, 2, 4, 5, 6, 3)).reshape(per_dest, parts, NBINS, nights, parts, -1)
    w_high = w.astype(jnp.bfloat16)
    w_low = (w - w_high.astype(jnp.float32)).astype(jnp.bfloat16)

    sums = None
    for n in range(nights):
        moved = lax.all_to_all(visibility[n], ("bl", "night"), split_axis=1, concat_axis=0, tiled=True)
        filtered = jnp.einsum("xbpc,cd->xbpd", moved, delay_filter,
                              preferred_element_type=jnp.float32).astype(jnp.bfloat16)
        part = jnp.einsum("bojpx,xbpc->jboc", w_high[:, :, :, n], filtered,
                          preferred_element_type=jnp.float32)
        part = part + jnp.einsum("bojpx,xbpc->jboc", w_low[:, :, :, n], filtered,
                                 preferred_element_type=jnp.float32)
        sums = part if sums is None else sums + part
    block = NBINS // groups
    lst_sums = jnp.zeros((block, groups * per_dest) + sums.shape[2:], sums.dtype)
    for shift in range(groups):
        target = (group + shift) % groups
        source = (group - shift) % groups
        piece = lax.dynamic_slice_in_dim(sums, target * block, block, axis=0)
        if shift:
            pairs = [(a, (a + shift) % groups) for a in range(groups)]
            piece = lax.ppermute(piece, "night", pairs)
        lst_sums = lax.dynamic_update_slice_in_dim(lst_sums, piece, source * per_dest, axis=1)

    times = all_bins.shape[1]
    j = jnp.arange(NBINS, dtype=jnp.int32)[:, None, None]
    s = jnp.arange(times, dtype=jnp.int32)[None, None, :]
    place = (j - all_bins[:, 0][None, :, None] == s).astype(jnp.float32)
    full_count = jnp.einsum("jns,nsb->jb", place, all_flags.astype(jnp.float32),
                            precision=lax.Precision.HIGHEST)
    counts = lax.dynamic_slice_in_dim(full_count, group * block, block, axis=0)
    lst_mean = lst_sums / jnp.maximum(counts, 1.0)[:, :, None, None]
    return (lst_mean, counts)


def solution(mesh):
    in_specs = (
        P("night", "bl", None, None, None),
        P(),
        P("bl", None, None),
        P("night", None),
        P("night", None, "bl"),
    )
    out_specs = (P("night", "bl", None, None), P("night", "bl"))
    return jax.shard_map(
        per_device, mesh=mesh, in_specs=in_specs, out_specs=out_specs, check_vma=False
    )
```

```python
import jax
import jax.numpy as jnp
from jax import lax
from jax.sharding import PartitionSpec as P

NBINS = 80
HALVES = 1


def smoothing_matrix(fringe_taps, lst_bin, flag_mask):
    nights = lst_bin.shape[0]
    times = lst_bin.shape[1]
    taps = fringe_taps.shape[2]
    half_taps = taps // 2
    start = lst_bin[:, 0]
    j = jnp.arange(NBINS, dtype=jnp.int32)[:, None, None]
    s = jnp.arange(times, dtype=jnp.int32)[None, None, :]
    t = j - start[None, :, None]
    k = s - t + half_taps
    inside = (t >= 0) & (t < times)
    onehot = ((k[..., None] == jnp.arange(taps, dtype=jnp.int32)) & inside[..., None]).astype(jnp.float32)
    h = jnp.einsum("jnsk,bqk->bqjns", onehot, fringe_taps, precision=lax.Precision.HIGHEST)
    hr = h[:, 0]
    hi = h[:, 1]
    row_real = jnp.stack([hr, -hi], axis=3)
    row_imag = jnp.stack([hi, hr], axis=3)
    w = jnp.stack([row_real, row_imag], axis=1)
    flags = jnp.transpose(flag_mask.astype(jnp.float32), (2, 0, 1))
    w = w * flags[:, None, None, :, None, :]
    return w


def exchange(sums, group, groups, per_dest):
    block = NBINS // groups
    out = jnp.zeros((block, groups * per_dest) + sums.shape[2:], jnp.float32)
    for shift in range(groups):
        target = (group + shift) % groups
        source = (group - shift) % groups
        piece = lax.dynamic_slice_in_dim(sums, target * block, block, axis=0)
        if shift:
            pairs = [(a, (a + shift) % groups) for a in range(groups)]
            piece = lax.ppermute(piece.astype(jnp.bfloat16), "night", pairs)
        out = lax.dynamic_update_slice_in_dim(out, piece.astype(jnp.float32), source * per_dest, axis=1)
    return out


def per_device(visibility, delay_filter, fringe_taps, lst_bin, flag_mask):
    nights, _, total_bl, parts, channels = visibility.shape
    groups = lax.psum(1, "night")
    bl_size = lax.psum(1, "bl")
    group = lax.axis_index("night")
    per_dest = total_bl // (groups * bl_size)

    all_bins = lax.all_gather(lst_bin, "night", axis=0, tiled=True)
    all_flags = lax.all_gather(flag_mask, "night", axis=0, tiled=True)
    own_flags = lax.dynamic_slice_in_dim(all_flags, group * per_dest, per_dest, axis=2)
    own_taps = lax.dynamic_slice_in_dim(fringe_taps, group * per_dest, per_dest, axis=0)
    w = smoothing_matrix(own_taps, all_bins, own_flags)
    w = w.reshape(per_dest, parts, NBINS, groups, nights, parts, bl_size)
    w = jnp.transpose(w, (0, 1, 2, 4, 5, 6, 3)).reshape(per_dest, parts, NBINS, nights, parts, -1)
    w_high = w.astype(jnp.bfloat16)
    w_low = (w - w_high.astype(jnp.float32)).astype(jnp.bfloat16)

    def smooth(n, moved, filt):
        filtered = jnp.einsum("xbpc,cd->xbpd", moved, filt,
                              preferred_element_type=jnp.float32).astype(jnp.bfloat16)
        part = jnp.einsum("bojpx,xbpc->jboc", w_high[:, :, :, n], filtered,
                          preferred_element_type=jnp.float32)
        return part + jnp.einsum("bojpx,xbpc->jboc", w_low[:, :, :, n], filtered,
                                 preferred_element_type=jnp.float32)

    moved = [lax.all_to_all(visibility[n], ("bl", "night"), split_axis=1, concat_axis=0, tiled=True)
             for n in range(nights)]
    early = None
    for n in range(nights - 1):
        part = smooth(n, moved[n], delay_filter)
        early = part if early is None else early + part
    width = channels // HALVES
    pieces = []
    for h in range(HALVES):
        filt = lax.slice_in_dim(delay_filter, h * width, (h + 1) * width, axis=1)
        sums = smooth(nights - 1, moved[nights - 1], filt)
        if early is not None:
            sums = sums + lax.slice_in_dim(early, h * width, (h + 1) * width, axis=3)
        pieces.append(exchange(sums, group, groups, per_dest))
    lst_sums = jnp.concatenate(pieces, axis=3)

    times = all_bins.shape[1]
    j = jnp.arange(NBINS, dtype=jnp.int32)[:, None, None]
    s = jnp.arange(times, dtype=jnp.int32)[None, None, :]
    place = (j - all_bins[:, 0][None, :, None] == s).astype(jnp.float32)
    full_count = jnp.einsum("jns,nsb->jb", place, all_flags.astype(jnp.float32),
                            precision=lax.Precision.HIGHEST)
    block = NBINS // groups
    counts = lax.dynamic_slice_in_dim(full_count, group * block, block, axis=0)
    lst_mean = lst_sums / jnp.maximum(counts, 1.0)[:, :, None, None]
    return (lst_mean, counts)


def solution(mesh):
    in_specs = (
        P("night", "bl", None, None, None),
        P(),
        P("bl", None, None),
        P("night", None),
        P("night", None, "bl"),
    )
    out_specs = (P("night", "bl", None, None), P("night", "bl"))
    return jax.shard_map(
        per_device, mesh=mesh, in_specs=in_specs, out_specs=out_specs, check_vma=False
    )
```

```python
import jax
import jax.numpy as jnp
from jax import lax
from jax.sharding import PartitionSpec as P

NBINS = 80


def smoothing_matrix(fringe_taps, lst_bin, flag_mask):
    nights = lst_bin.shape[0]
    times = lst_bin.shape[1]
    taps = fringe_taps.shape[2]
    half_taps = taps // 2
    start = lst_bin[:, 0]
    j = jnp.arange(NBINS, dtype=jnp.int32)[:, None, None]
    s = jnp.arange(times, dtype=jnp.int32)[None, None, :]
    t = j - start[None, :, None]
    k = s - t + half_taps
    inside = (t >= 0) & (t < times)
    onehot = ((k[..., None] == jnp.arange(taps, dtype=jnp.int32)) & inside[..., None]).astype(jnp.float32)
    h = jnp.einsum("jnsk,bqk->bqjns", onehot, fringe_taps, precision=lax.Precision.HIGHEST)
    hr = h[:, 0]
    hi = h[:, 1]
    row_real = jnp.stack([hr, -hi], axis=3)
    row_imag = jnp.stack([hi, hr], axis=3)
    w = jnp.stack([row_real, row_imag], axis=1)
    flags = jnp.transpose(flag_mask.astype(jnp.float32), (2, 0, 1))
    w = w * flags[:, None, None, :, None, :]
    return w


def exchange(sums, group, groups, per_dest):
    block = NBINS // groups
    out = jnp.zeros((block, groups * per_dest) + sums.shape[2:], sums.dtype)
    for shift in range(groups):
        target = (group + shift) % groups
        source = (group - shift) % groups
        piece = lax.dynamic_slice_in_dim(sums, target * block, block, axis=0)
        if shift:
            pairs = [(a, (a + shift) % groups) for a in range(groups)]
            piece = lax.ppermute(piece, "night", pairs)
        out = lax.dynamic_update_slice_in_dim(out, piece, source * per_dest, axis=1)
    return out


def per_device(visibility, delay_filter, fringe_taps, lst_bin, flag_mask):
    nights, _, total_bl, parts, channels = visibility.shape
    groups = lax.psum(1, "night")
    bl_size = lax.psum(1, "bl")
    group = lax.axis_index("night")
    per_dest = total_bl // (groups * bl_size)

    moved = lax.all_to_all(visibility, ("bl", "night"), split_axis=2, concat_axis=1, tiled=True)

    all_bins = lax.all_gather(lst_bin, "night", axis=0, tiled=True)
    all_flags = lax.all_gather(flag_mask, "night", axis=0, tiled=True)
    own_flags = lax.dynamic_slice_in_dim(all_flags, group * per_dest, per_dest, axis=2)
    own_taps = lax.dynamic_slice_in_dim(fringe_taps, group * per_dest, per_dest, axis=0)
    w = smoothing_matrix(own_taps, all_bins, own_flags)
    w = w.reshape(per_dest, parts, NBINS, groups, nights, parts, bl_size)
    w = jnp.transpose(w, (0, 1, 2, 4, 5, 6, 3)).reshape(per_dest, parts, NBINS, nights, parts, -1)
    w_high = w.astype(jnp.bfloat16)
    w_low = (w - w_high.astype(jnp.float32)).astype(jnp.bfloat16)

    binned = jnp.einsum("bojnpx,nxbpc->jboc", w_high, moved, preferred_element_type=jnp.float32)
    binned = binned + jnp.einsum("bojnpx,nxbpc->jboc", w_low, moved, preferred_element_type=jnp.float32)
    binned = exchange(binned.astype(jnp.bfloat16), group, groups, per_dest)
    lst_sums = jnp.einsum("jbpc,cd->jbpd", binned, delay_filter, preferred_element_type=jnp.float32)

    times = all_bins.shape[1]
    j = jnp.arange(NBINS, dtype=jnp.int32)[:, None, None]
    s = jnp.arange(times, dtype=jnp.int32)[None, None, :]
    place = (j - all_bins[:, 0][None, :, None] == s).astype(jnp.float32)
    full_count = jnp.einsum("jns,nsb->jb", place, all_flags.astype(jnp.float32),
                            precision=lax.Precision.HIGHEST)
    block = NBINS // groups
    counts = lax.dynamic_slice_in_dim(full_count, group * block, block, axis=0)
    lst_mean = lst_sums / jnp.maximum(counts, 1.0)[:, :, None, None]
    return (lst_mean, counts)


def solution(mesh):
    in_specs = (
        P("night", "bl", None, None, None),
        P(),
        P("bl", None, None),
        P("night", None),
        P("night", None, "bl"),
    )
    out_specs = (P("night", "bl", None, None), P("night", "bl"))
    return jax.shard_map(
        per_device, mesh=mesh, in_specs=in_specs, out_specs=out_specs, check_vma=False
    )
```

```python
import jax
import jax.numpy as jnp
from jax import lax
from jax.sharding import PartitionSpec as P

NBINS = 80


def smoothing_matrix(fringe_taps, lst_bin, flag_mask):
    nights = lst_bin.shape[0]
    times = lst_bin.shape[1]
    taps = fringe_taps.shape[2]
    half_taps = taps // 2
    start = lst_bin[:, 0]
    j = jnp.arange(NBINS, dtype=jnp.int32)[:, None, None]
    s = jnp.arange(times, dtype=jnp.int32)[None, None, :]
    t = j - start[None, :, None]
    k = s - t + half_taps
    inside = (t >= 0) & (t < times)
    onehot = ((k[..., None] == jnp.arange(taps, dtype=jnp.int32)) & inside[..., None]).astype(jnp.float32)
    h = jnp.einsum("jnsk,bqk->bqjns", onehot, fringe_taps, precision=lax.Precision.HIGHEST)
    hr = h[:, 0]
    hi = h[:, 1]
    row_real = jnp.stack([hr, -hi], axis=3)
    row_imag = jnp.stack([hi, hr], axis=3)
    w = jnp.stack([row_real, row_imag], axis=1)
    flags = jnp.transpose(flag_mask.astype(jnp.float32), (2, 0, 1))
    w = w * flags[:, None, None, :, None, :]
    return w


def exchange(sums, group, groups, per_dest):
    block = NBINS // groups
    out = jnp.zeros((block, groups * per_dest) + sums.shape[2:], sums.dtype)
    for shift in range(groups):
        target = (group + shift) % groups
        source = (group - shift) % groups
        piece = lax.dynamic_slice_in_dim(sums, target * block, block, axis=0)
        if shift:
            pairs = [(a, (a + shift) % groups) for a in range(groups)]
            piece = lax.ppermute(piece, "night", pairs)
        out = lax.dynamic_update_slice_in_dim(out, piece, source * per_dest, axis=1)
    return out


def per_device(visibility, delay_filter, fringe_taps, lst_bin, flag_mask):
    nights, _, total_bl, parts, channels = visibility.shape
    groups = lax.psum(1, "night")
    bl_size = lax.psum(1, "bl")
    group = lax.axis_index("night")
    per_dest = total_bl // (groups * bl_size)

    moved = lax.all_to_all(visibility, ("bl", "night"), split_axis=2, concat_axis=1, tiled=True)

    all_bins = lax.all_gather(lst_bin, "night", axis=0, tiled=True)
    all_flags = lax.all_gather(flag_mask, "night", axis=0, tiled=True)
    own_flags = lax.dynamic_slice_in_dim(all_flags, group * per_dest, per_dest, axis=2)
    own_taps = lax.dynamic_slice_in_dim(fringe_taps, group * per_dest, per_dest, axis=0)
    w = smoothing_matrix(own_taps, all_bins, own_flags)
    w = w.reshape(per_dest, parts, NBINS, groups, nights, parts, bl_size)
    w = jnp.transpose(w, (0, 1, 2, 4, 5, 6, 3)).reshape(per_dest, parts, NBINS, nights, parts, -1)
    w_high = w.astype(jnp.bfloat16)
    w_low = (w - w_high.astype(jnp.float32)).astype(jnp.bfloat16)

    w_split = jnp.stack([w_high, w_low], axis=1)
    binned = jnp.einsum("bhojnpx,nxbpc->jbhoc", w_split, moved, preferred_element_type=jnp.float32)
    binned = binned[:, :, 0] + binned[:, :, 1]
    binned = exchange(binned.astype(jnp.bfloat16), group, groups, per_dest)
    lst_sums = jnp.einsum("jbpc,cd->jbpd", binned, delay_filter, preferred_element_type=jnp.float32)

    times = all_bins.shape[1]
    j = jnp.arange(NBINS, dtype=jnp.int32)[:, None, None]
    s = jnp.arange(times, dtype=jnp.int32)[None, None, :]
    place = (j - all_bins[:, 0][None, :, None] == s).astype(jnp.float32)
    full_count = jnp.einsum("jns,nsb->jb", place, all_flags.astype(jnp.float32),
                            precision=lax.Precision.HIGHEST)
    block = NBINS // groups
    counts = lax.dynamic_slice_in_dim(full_count, group * block, block, axis=0)
    lst_mean = lst_sums / jnp.maximum(counts, 1.0)[:, :, None, None]
    return (lst_mean, counts)


def solution(mesh):
    in_specs = (
        P("night", "bl", None, None, None),
        P(),
        P("bl", None, None),
        P("night", None),
        P("night", None, "bl"),
    )
    out_specs = (P("night", "bl", None, None), P("night", "bl"))
    return jax.shard_map(
        per_device, mesh=mesh, in_specs=in_specs, out_specs=out_specs, check_vma=False
    )
```

```python
import jax
import jax.numpy as jnp
from jax import lax
from jax.sharding import PartitionSpec as P

NBINS = 80


def smoothing_matrix(fringe_taps, lst_bin, flag_mask):
    nights = lst_bin.shape[0]
    times = lst_bin.shape[1]
    taps = fringe_taps.shape[2]
    half_taps = taps // 2
    start = lst_bin[:, 0]
    j = jnp.arange(NBINS, dtype=jnp.int32)[:, None, None]
    s = jnp.arange(times, dtype=jnp.int32)[None, None, :]
    t = j - start[None, :, None]
    k = s - t + half_taps
    inside = (t >= 0) & (t < times)
    onehot = ((k[..., None] == jnp.arange(taps, dtype=jnp.int32)) & inside[..., None]).astype(jnp.float32)
    h = jnp.einsum("jnsk,bqk->bqjns", onehot, fringe_taps, precision=lax.Precision.HIGHEST)
    hr = h[:, 0]
    hi = h[:, 1]
    row_real = jnp.stack([hr, -hi], axis=3)
    row_imag = jnp.stack([hi, hr], axis=3)
    w = jnp.stack([row_real, row_imag], axis=1)
    flags = jnp.transpose(flag_mask.astype(jnp.float32), (2, 0, 1))
    w = w * flags[:, None, None, :, None, :]
    return w


def per_device(visibility, delay_filter, fringe_taps, lst_bin, flag_mask):
    nights, _, total_bl, parts, channels = visibility.shape
    groups = lax.psum(1, "night")
    bl_size = lax.psum(1, "bl")
    group = lax.axis_index("night")
    per_dest = total_bl // (groups * bl_size)

    moved = lax.all_to_all(visibility, ("bl", "night"), split_axis=2, concat_axis=1, tiled=True)

    all_bins = lax.all_gather(lst_bin, "night", axis=0, tiled=True)
    all_flags = lax.all_gather(flag_mask, "night", axis=0, tiled=True)
    own_flags = lax.dynamic_slice_in_dim(all_flags, group * per_dest, per_dest, axis=2)
    own_taps = lax.dynamic_slice_in_dim(fringe_taps, group * per_dest, per_dest, axis=0)
    w = smoothing_matrix(own_taps, all_bins, own_flags)
    w = w.reshape(per_dest, parts, NBINS, groups, nights, parts, bl_size)
    w = jnp.transpose(w, (0, 1, 2, 4, 5, 6, 3)).reshape(per_dest, parts, NBINS, nights, parts, -1)
    w_high = w.astype(jnp.bfloat16)
    w_low = (w - w_high.astype(jnp.float32)).astype(jnp.bfloat16)

    w_split = jnp.stack([w_high, w_low], axis=1)
    block = NBINS // groups

    def binned_rows(first_device):
        rows = lax.dynamic_slice_in_dim(w_split, first_device * block, 2 * block, axis=3)
        out = jnp.einsum("bhojnpx,nxbpc->jbhoc", rows, moved, preferred_element_type=jnp.float32)
        return (out[:, :, 0] + out[:, :, 1]).astype(jnp.bfloat16)

    own_chip = group - group % 2
    other_chip = (own_chip + 2) % groups
    binned = jnp.zeros((block, groups * per_dest, parts, channels), jnp.bfloat16)
    for first_device, shifts in ((other_chip, (2, 3)), (own_chip, (0, 1))):
        rows = binned_rows(first_device)
        for shift in shifts:
            partner = jnp.bitwise_xor(group, shift)
            piece = lax.dynamic_slice_in_dim(rows, (partner - first_device) * block, block, axis=0)
            if shift:
                pairs = [(a, a ^ shift) for a in range(groups)]
                piece = lax.ppermute(piece, "night", pairs)
            binned = lax.dynamic_update_slice_in_dim(binned, piece, partner * per_dest, axis=1)
    lst_sums = jnp.einsum("jbpc,cd->jbpd", binned, delay_filter, preferred_element_type=jnp.float32)

    times = all_bins.shape[1]
    j = jnp.arange(NBINS, dtype=jnp.int32)[:, None, None]
    s = jnp.arange(times, dtype=jnp.int32)[None, None, :]
    place = (j - all_bins[:, 0][None, :, None] == s).astype(jnp.float32)
    full_count = jnp.einsum("jns,nsb->jb", place, all_flags.astype(jnp.float32),
                            precision=lax.Precision.HIGHEST)
    counts = lax.dynamic_slice_in_dim(full_count, group * block, block, axis=0)
    lst_mean = lst_sums / jnp.maximum(counts, 1.0)[:, :, None, None]
    return (lst_mean, counts)


def solution(mesh):
    in_specs = (
        P("night", "bl", None, None, None),
        P(),
        P("bl", None, None),
        P("night", None),
        P("night", None, "bl"),
    )
    out_specs = (P("night", "bl", None, None), P("night", "bl"))
    return jax.shard_map(
        per_device, mesh=mesh, in_specs=in_specs, out_specs=out_specs, check_vma=False
    )
```

```python
import jax
import jax.numpy as jnp
from jax import lax
from jax.sharding import PartitionSpec as P

NBINS = 80


def smoothing_matrix(fringe_taps, lst_bin, flag_mask):
    nights = lst_bin.shape[0]
    times = lst_bin.shape[1]
    taps = fringe_taps.shape[2]
    half_taps = taps // 2
    start = lst_bin[:, 0]
    j = jnp.arange(NBINS, dtype=jnp.int32)[:, None, None]
    s = jnp.arange(times, dtype=jnp.int32)[None, None, :]
    t = j - start[None, :, None]
    k = s - t + half_taps
    inside = (t >= 0) & (t < times)
    onehot = ((k[..., None] == jnp.arange(taps, dtype=jnp.int32)) & inside[..., None]).astype(jnp.float32)
    h = jnp.einsum("jnsk,bqk->bqjns", onehot, fringe_taps, precision=lax.Precision.HIGHEST)
    hr = h[:, 0]
    hi = h[:, 1]
    row_real = jnp.stack([hr, -hi], axis=3)
    row_imag = jnp.stack([hi, hr], axis=3)
    w = jnp.stack([row_real, row_imag], axis=1)
    flags = jnp.transpose(flag_mask.astype(jnp.float32), (2, 0, 1))
    w = w * flags[:, None, None, :, None, :]
    return w


def per_device(visibility, delay_filter, fringe_taps, lst_bin, flag_mask):
    nights, _, total_bl, parts, channels = visibility.shape
    groups = lax.psum(1, "night")
    bl_size = lax.psum(1, "bl")
    group = lax.axis_index("night")
    per_dest = total_bl // (groups * bl_size)

    moved = lax.all_to_all(visibility, ("bl", "night"), split_axis=2, concat_axis=1, tiled=True)
    filtered = jnp.einsum("nxbpc,cd->nxbpd", moved, delay_filter,
                          preferred_element_type=jnp.float32).astype(jnp.bfloat16)

    all_bins = lax.all_gather(lst_bin, "night", axis=0, tiled=True)
    all_flags = lax.all_gather(flag_mask, "night", axis=0, tiled=True)
    own_flags = lax.dynamic_slice_in_dim(all_flags, group * per_dest, per_dest, axis=2)
    own_taps = lax.dynamic_slice_in_dim(fringe_taps, group * per_dest, per_dest, axis=0)
    w = smoothing_matrix(own_taps, all_bins, own_flags)
    w = w.reshape(per_dest, parts, NBINS, groups, nights, parts, bl_size)
    w = jnp.transpose(w, (0, 1, 2, 4, 5, 6, 3)).reshape(per_dest, parts, NBINS, nights, parts, -1)
    w_high = w.astype(jnp.bfloat16)
    w_low = (w - w_high.astype(jnp.float32)).astype(jnp.bfloat16)

    w_split = jnp.stack([w_high, w_low], axis=1)
    block = NBINS // groups

    sums = jnp.einsum("bhojnpx,nxbpc->jbhoc", w_split, filtered, preferred_element_type=jnp.float32)
    sums = sums[:, :, 0] + sums[:, :, 1]
    lst_sums = jnp.zeros((block, groups * per_dest, parts, channels), jnp.float32)
    for shift in range(groups):
        target = (group + shift) % groups
        source = (group - shift) % groups
        piece = lax.dynamic_slice_in_dim(sums, target * block, block, axis=0)
        if shift:
            pairs = [(a, (a + shift) % groups) for a in range(groups)]
            piece = lax.ppermute(piece.astype(jnp.bfloat16), "night", pairs).astype(jnp.float32)
        lst_sums = lax.dynamic_update_slice_in_dim(lst_sums, piece, source * per_dest, axis=1)

    times = all_bins.shape[1]
    j = jnp.arange(NBINS, dtype=jnp.int32)[:, None, None]
    s = jnp.arange(times, dtype=jnp.int32)[None, None, :]
    place = (j - all_bins[:, 0][None, :, None] == s).astype(jnp.float32)
    full_count = jnp.einsum("jns,nsb->jb", place, all_flags.astype(jnp.float32),
                            precision=lax.Precision.HIGHEST)
    counts = lax.dynamic_slice_in_dim(full_count, group * block, block, axis=0)
    lst_mean = lst_sums / jnp.maximum(counts, 1.0)[:, :, None, None]
    return (lst_mean, counts)


def solution(mesh):
    in_specs = (
        P("night", "bl", None, None, None),
        P(),
        P("bl", None, None),
        P("night", None),
        P("night", None, "bl"),
    )
    out_specs = (P("night", "bl", None, None), P("night", "bl"))
    return jax.shard_map(
        per_device, mesh=mesh, in_specs=in_specs, out_specs=out_specs, check_vma=False
    )
```

```python
import jax
import jax.numpy as jnp
from jax import lax
from jax.sharding import PartitionSpec as P

NBINS = 80


def smoothing_matrix(fringe_taps, lst_bin, flag_mask):
    nights = lst_bin.shape[0]
    times = lst_bin.shape[1]
    taps = fringe_taps.shape[2]
    half_taps = taps // 2
    start = lst_bin[:, 0]
    j = jnp.arange(NBINS, dtype=jnp.int32)[:, None, None]
    s = jnp.arange(times, dtype=jnp.int32)[None, None, :]
    t = j - start[None, :, None]
    k = s - t + half_taps
    inside = (t >= 0) & (t < times)
    onehot = ((k[..., None] == jnp.arange(taps, dtype=jnp.int32)) & inside[..., None]).astype(jnp.float32)
    h = jnp.einsum("jnsk,bqk->bqjns", onehot, fringe_taps, precision=lax.Precision.HIGHEST)
    hr = h[:, 0]
    hi = h[:, 1]
    row_real = jnp.stack([hr, -hi], axis=3)
    row_imag = jnp.stack([hi, hr], axis=3)
    w = jnp.stack([row_real, row_imag], axis=1)
    flags = jnp.transpose(flag_mask.astype(jnp.float32), (2, 0, 1))
    w = w * flags[:, None, None, :, None, :]
    return w


def per_device(visibility, delay_filter, fringe_taps, lst_bin, flag_mask):
    nights, _, total_bl, parts, channels = visibility.shape
    groups = lax.psum(1, "night")
    bl_size = lax.psum(1, "bl")
    group = lax.axis_index("night")
    per_dest = total_bl // (groups * bl_size)

    moved = lax.all_to_all(visibility, ("bl", "night"), split_axis=2, concat_axis=1, tiled=True)
    filtered = jnp.einsum("nxbpc,cd->nxbpd", moved, delay_filter,
                          preferred_element_type=jnp.float32).astype(jnp.bfloat16)

    all_bins = lax.all_gather(lst_bin, "night", axis=0, tiled=True)
    all_flags = lax.all_gather(flag_mask, "night", axis=0, tiled=True)
    own_flags = lax.dynamic_slice_in_dim(all_flags, group * per_dest, per_dest, axis=2)
    own_taps = lax.dynamic_slice_in_dim(fringe_taps, group * per_dest, per_dest, axis=0)
    w = smoothing_matrix(own_taps, all_bins, own_flags)
    w = w.reshape(per_dest, parts, NBINS, groups, nights, parts, bl_size)
    w = jnp.transpose(w, (0, 1, 2, 4, 5, 6, 3)).reshape(per_dest, parts, NBINS, nights, parts, -1)
    w_high = w.astype(jnp.bfloat16)
    w_low = (w - w_high.astype(jnp.float32)).astype(jnp.bfloat16)

    w_split = jnp.stack([w_high, w_low], axis=1)
    block = NBINS // groups

    sums = jnp.einsum("bhojnpx,nxbpc->jbhoc", w_split, filtered, preferred_element_type=jnp.float32)
    sums = sums[:, :, 0] + sums[:, :, 1]
    times = all_bins.shape[1]
    j = jnp.arange(NBINS, dtype=jnp.int32)[:, None, None]
    s = jnp.arange(times, dtype=jnp.int32)[None, None, :]
    place = (j - all_bins[:, 0][None, :, None] == s).astype(jnp.float32)
    full_count = jnp.einsum("jns,nsb->jb", place, all_flags.astype(jnp.float32),
                            precision=lax.Precision.HIGHEST)
    counts = lax.dynamic_slice_in_dim(full_count, group * block, block, axis=0)
    divisor = jnp.maximum(counts, 1.0)
    lst_sums = jnp.zeros((block, groups * per_dest, parts, channels), jnp.float32)
    for shift in range(groups):
        target = (group + shift) % groups
        source = (group - shift) % groups
        piece = lax.dynamic_slice_in_dim(sums, target * block, block, axis=0)
        if shift:
            pairs = [(a, (a + shift) % groups) for a in range(groups)]
            piece = lax.ppermute(piece.astype(jnp.bfloat16), "night", pairs).astype(jnp.float32)
        scale = lax.dynamic_slice_in_dim(divisor, source * per_dest, per_dest, axis=1)
        piece = piece / scale[:, :, None, None]
        lst_sums = lax.dynamic_update_slice_in_dim(lst_sums, piece, source * per_dest, axis=1)

    lst_mean = lst_sums
    return (lst_mean, counts)


def solution(mesh):
    in_specs = (
        P("night", "bl", None, None, None),
        P(),
        P("bl", None, None),
        P("night", None),
        P("night", None, "bl"),
    )
    out_specs = (P("night", "bl", None, None), P("night", "bl"))
    return jax.shard_map(
        per_device, mesh=mesh, in_specs=in_specs, out_specs=out_specs, check_vma=False
    )
```

```python
import jax
import jax.numpy as jnp
from jax import lax
from jax.sharding import PartitionSpec as P

NBINS = 80
SHIFT_ORDER = (2, 1, 3, 0)


def smoothing_matrix(fringe_taps, lst_bin, flag_mask):
    nights = lst_bin.shape[0]
    times = lst_bin.shape[1]
    taps = fringe_taps.shape[2]
    half_taps = taps // 2
    start = lst_bin[:, 0]
    j = jnp.arange(NBINS, dtype=jnp.int32)[:, None, None]
    s = jnp.arange(times, dtype=jnp.int32)[None, None, :]
    t = j - start[None, :, None]
    k = s - t + half_taps
    inside = (t >= 0) & (t < times)
    onehot = ((k[..., None] == jnp.arange(taps, dtype=jnp.int32)) & inside[..., None]).astype(jnp.float32)
    h = jnp.einsum("jnsk,bqk->bqjns", onehot, fringe_taps, precision=lax.Precision.HIGHEST)
    hr = h[:, 0]
    hi = h[:, 1]
    row_real = jnp.stack([hr, -hi], axis=3)
    row_imag = jnp.stack([hi, hr], axis=3)
    w = jnp.stack([row_real, row_imag], axis=1)
    flags = jnp.transpose(flag_mask.astype(jnp.float32), (2, 0, 1))
    w = w * flags[:, None, None, :, None, :]
    return w


def per_device(visibility, delay_filter, fringe_taps, lst_bin, flag_mask):
    nights, _, total_bl, parts, channels = visibility.shape
    groups = lax.psum(1, "night")
    bl_size = lax.psum(1, "bl")
    group = lax.axis_index("night")
    per_dest = total_bl // (groups * bl_size)

    moved = lax.all_to_all(visibility, ("bl", "night"), split_axis=2, concat_axis=1, tiled=True)
    filtered = jnp.einsum("nxbpc,cd->nxbpd", moved, delay_filter,
                          preferred_element_type=jnp.float32).astype(jnp.bfloat16)

    all_bins = lax.all_gather(lst_bin, "night", axis=0, tiled=True)
    all_flags = lax.all_gather(flag_mask, "night", axis=0, tiled=True)
    own_flags = lax.dynamic_slice_in_dim(all_flags, group * per_dest, per_dest, axis=2)
    own_taps = lax.dynamic_slice_in_dim(fringe_taps, group * per_dest, per_dest, axis=0)
    w = smoothing_matrix(own_taps, all_bins, own_flags)
    w = w.reshape(per_dest, parts, NBINS, groups, nights, parts, bl_size)
    w = jnp.transpose(w, (0, 1, 2, 4, 5, 6, 3)).reshape(per_dest, parts, NBINS, nights, parts, -1)
    w_high = w.astype(jnp.bfloat16)
    w_low = (w - w_high.astype(jnp.float32)).astype(jnp.bfloat16)

    w_split = jnp.stack([w_high, w_low], axis=1)
    block = NBINS // groups

    sums = jnp.einsum("bhojnpx,nxbpc->jbhoc", w_split, filtered, preferred_element_type=jnp.float32)
    sums = sums[:, :, 0] + sums[:, :, 1]
    times = all_bins.shape[1]
    j = jnp.arange(NBINS, dtype=jnp.int32)[:, None, None]
    s = jnp.arange(times, dtype=jnp.int32)[None, None, :]
    place = (j - all_bins[:, 0][None, :, None] == s).astype(jnp.float32)
    full_count = jnp.einsum("jns,nsb->jb", place, all_flags.astype(jnp.float32),
                            precision=lax.Precision.HIGHEST)
    counts = lax.dynamic_slice_in_dim(full_count, group * block, block, axis=0)
    divisor = jnp.maximum(counts, 1.0)
    lst_sums = jnp.zeros((block, groups * per_dest, parts, channels), jnp.float32)
    for shift in SHIFT_ORDER:
        target = (group + shift) % groups
        source = (group - shift) % groups
        piece = lax.dynamic_slice_in_dim(sums, target * block, block, axis=0)
        if shift:
            pairs = [(a, (a + shift) % groups) for a in range(groups)]
            piece = lax.ppermute(piece.astype(jnp.bfloat16), "night", pairs).astype(jnp.float32)
        scale = lax.dynamic_slice_in_dim(divisor, source * per_dest, per_dest, axis=1)
        piece = piece / scale[:, :, None, None]
        lst_sums = lax.dynamic_update_slice_in_dim(lst_sums, piece, source * per_dest, axis=1)

    lst_mean = lst_sums
    return (lst_mean, counts)


def solution(mesh):
    in_specs = (
        P("night", "bl", None, None, None),
        P(),
        P("bl", None, None),
        P("night", None),
        P("night", None, "bl"),
    )
    out_specs = (P("night", "bl", None, None), P("night", "bl"))
    return jax.shard_map(
        per_device, mesh=mesh, in_specs=in_specs, out_specs=out_specs, check_vma=False
    )
```
